1024 devices in a mesh: box: 128 (over x, y, core), ang: 8 (over z).
Axes of the slice: x: 8, y: 8, z: 8, core: 2. Of those that a mesh axis runs over, the one named last changes fastest.
Arguments:
- children: bfloat16 [131072, 2, 1024], P(('box', 'ang')), may hold values from -6 to 6
- interp_band: float32 [2048, 6], replicated, may hold values from -0.5 to 1
- band_start: int32 [2048], replicated, may hold values from 0 to 1018, as said below
- shift_angle: float32 [8, 2048], replicated, may hold values from -3.140625 to 3.140625
- far_box: int32 [16384, 27], P('box'), may hold values from 0 to 16383, as said below
- far_class: int32 [16384, 27], P('box'), may hold values from 0 to 315
- far_count: int32 [16384], P('box'), may hold values from 9 to 27, as said below
- translation: float32 [316, 2, 2048], replicated, may hold values from -0.3 to 0.3
Outputs:
- local_field: float32 [131072, 2, 1024], P(('box', 'ang'))
The draws below stay inside these ranges and needn't reach their ends.
Inputs may be any that keep to these rules, and one draw needn't show every extreme that they name: `band_start`: every band lies inside the child-level samples. far_box[p, l] differs from p by 2 to 16. `far_count`: each aligned block of 128 parents (the parents of one index of box) holds at least one parent with all 27 slots live.
All inputs are finite; a program needn't handle non-finite values.
Results may differ from the reference program's by a relative error of at most 0.0063.
Values may be sent and summed in bfloat16 or wider, within the bound.
No kernel may reach another device: no remote copies, remote signals or barrier semaphores. Data moves between devices by JAX's collectives and lax.ppermute only.
A program may use at most 64 MiB of HBM per device.

```python
import jax
import jax.numpy as jnp
from jax import lax

K_LOW = 1024
K_HIGH = 2048
BAND = 6
NCLASS = 316
FAR = 27
REACH = 16
GROUP_BOXES = 128
PARENTS = 16384
CHILDREN = 131072


def draw_band_start(key, part):
    sample_ids = jnp.arange(K_HIGH, dtype=jnp.int32)
    jitter = jax.random.randint(jax.random.fold_in(key, 11), (K_HIGH,), 0, 2)
    return jnp.clip(sample_ids * K_LOW // K_HIGH - BAND // 2 + jitter, 0, K_LOW - BAND).astype(jnp.int32)


def draw_far_box(key, part):
    first_key = jax.random.fold_in(key, 21)
    second_key = jax.random.fold_in(key, 22)
    distance = jax.random.randint(first_key, (PARENTS, FAR), 2, REACH + 1)
    direction = 2 * jax.random.randint(second_key, (PARENTS, FAR), 0, 2) - 1
    owners = jnp.arange(PARENTS, dtype=jnp.int32)[:, None]
    target = owners + direction * distance
    outside = jnp.logical_or(target < 0, target >= PARENTS)
    return jnp.where(outside, owners - direction * distance, target).astype(jnp.int32)


def draw_far_count(key, part):
    base = jax.random.randint(jax.random.fold_in(key, 31), (PARENTS,), FAR // 3, FAR + 1)
    picked = jax.random.randint(jax.random.fold_in(key, 32), (PARENTS // GROUP_BOXES,), 0, GROUP_BOXES)
    positions = jnp.arange(GROUP_BOXES, dtype=jnp.int32)
    full_rows = (positions[None, :] == picked[:, None]).reshape(-1)
    return jnp.where(full_rows, FAR, base).astype(jnp.int32)


def touch_ends(array, own_key, smallest, high):
    longest = array.shape.index(max(array.shape))
    spots = []
    for shift in (0, 1):
        where = [jax.random.randint(jax.random.fold_in(own_key, axis), (), 0, length) for axis, length in enumerate(array.shape)]
        where[longest] = (where[longest] + shift) % array.shape[longest]
        spots.append(tuple(where))
    return array.at[spots[0]].set(smallest).at[spots[1]].set(high)


def block_levels(stream_key, extent, split, smallest, largest):
    factor_of, own = 1.0, jax.random.fold_in(stream_key, 6)
    for dim, blocks in split:
        steps = jnp.exp(jax.random.uniform(jax.random.fold_in(own, dim), (blocks,), jnp.float32, smallest / len(split), largest / len(split)))
        factor_of = factor_of * jnp.repeat(steps, extent[dim] // blocks).reshape([-1 if axis == dim else 1 for axis in range(len(extent))])
    return factor_of


def normal_values(key, shape, scale, reach, split=(), held_as=jnp.bfloat16):
    level = block_levels(key, shape, split, -0.22, 0.18) if split else 1.0
    entries = jax.random.normal(key, shape, jnp.float32) * scale * level
    return jnp.minimum(jnp.maximum(entries, -reach), reach).astype(held_as)


def setup_inputs(seed: int = 0) -> dict:
    streams_of = jax.random.split(jax.random.key(seed), 9)
    children = normal_values(streams_of[0], (CHILDREN, 2, K_LOW), 1.0, 6.0, ((0, 1024),))
    interp_band = jnp.clip(jax.random.uniform(streams_of[1], (K_HIGH, BAND), jnp.float32, -0.5, 1.0), -0.5, 1.0)
    band_start = draw_band_start(jax.random.fold_in(streams_of[8], 71), 0)
    shift_angle = jnp.clip(jax.random.uniform(streams_of[3], (8, K_HIGH), jnp.float32, -3.140625, 3.140625), -3.140625, 3.140625)
    far_box = draw_far_box(jax.random.fold_in(streams_of[8], 71), 0)
    far_class = touch_ends(jax.random.randint(streams_of[5], (PARENTS, FAR), 0, NCLASS), jax.random.fold_in(streams_of[5], 1), 0, NCLASS - 1).astype(jnp.int32)
    far_count = draw_far_count(jax.random.fold_in(streams_of[8], 71), 0)
    translation = normal_values(streams_of[7], (NCLASS, 2, K_HIGH), 0.05, 0.3, (), jnp.float32)
    return {"children": children, "interp_band": interp_band, "band_start": band_start, "shift_angle": shift_angle, "far_box": far_box, "far_class": far_class, "far_count": far_count, "translation": translation}


def build_interp(interp_band, band_start):
    low_ids = jnp.arange(K_LOW, dtype=jnp.int32)
    dense = jnp.zeros((K_LOW, K_HIGH), jnp.float32)
    for column in range(BAND):
        target = (band_start + column).astype(jnp.int32)
        dense = dense + jnp.where(low_ids[:, None] == target[None, :], interp_band[:, column][None, :], jnp.float32(0.0))
    return dense.astype(jnp.bfloat16)


def shift_up(values, cosines, sines):
    real_part = values[:, :, 0, :] * cosines - values[:, :, 1, :] * sines
    imag_part = values[:, :, 0, :] * sines + values[:, :, 1, :] * cosines
    return jnp.stack([real_part, imag_part], axis=2)


def shift_down(values, cosines, sines):
    real_in = values[:, None, 0, :]
    imag_in = values[:, None, 1, :]
    real_part = real_in * cosines + imag_in * sines
    imag_part = imag_in * cosines - real_in * sines
    return jnp.stack([real_part, imag_part], axis=2)


def translate(patterns, operators, targets, classes, counts):
    gathered = patterns[targets].astype(jnp.float32)
    chosen = operators[classes]
    slots = jnp.arange(classes.shape[1], dtype=jnp.int32)
    live = (slots[None, :] < counts[:, None]).astype(jnp.float32)[:, :, None]
    real_part = jnp.sum(live * (chosen[:, :, 0] * gathered[:, :, 0] - chosen[:, :, 1] * gathered[:, :, 1]), axis=1)
    imag_part = jnp.sum(live * (chosen[:, :, 0] * gathered[:, :, 1] + chosen[:, :, 1] * gathered[:, :, 0]), axis=1)
    return jnp.stack([real_part, imag_part], axis=1)


def reference(children, interp_band, band_start, shift_angle, far_box, far_class, far_count, translation):
    interp = build_interp(interp_band, band_start)
    raised = jnp.dot(children.reshape(-1, K_LOW), interp, preferred_element_type=jnp.float32)
    raised = raised.reshape(-1, 8, 2, K_HIGH)
    cosines = jnp.cos(shift_angle)
    sines = jnp.sin(shift_angle)
    parent = jnp.sum(shift_up(raised, cosines, sines), axis=1).astype(jnp.bfloat16)

    def one_group(items):
        return translate(parent, translation, items[0], items[1], items[2])

    groups = lax.map(one_group, (far_box.reshape(-1, GROUP_BOXES, FAR), far_class.reshape(-1, GROUP_BOXES, FAR), far_count.reshape(-1, GROUP_BOXES)))
    local = groups.reshape(PARENTS, 2, K_HIGH).astype(jnp.bfloat16)
    spread = shift_down(local.astype(jnp.float32), cosines, sines).astype(jnp.bfloat16)
    result = jnp.dot(spread.reshape(-1, K_HIGH), interp.T, preferred_element_type=jnp.float32)
    return result.reshape(-1, 2, K_LOW)
```

```python
import jax
import jax.numpy as jnp
from jax import lax
from jax.sharding import PartitionSpec as P

K_LOW = 1024
REACH = 16


def build_interp(interp_band, band_start):
    low_ids = jnp.arange(K_LOW, dtype=jnp.int32)
    dense = jnp.zeros((K_LOW, interp_band.shape[0]), jnp.float32)
    for column in range(interp_band.shape[1]):
        target = band_start + column
        dense = dense + jnp.where(
            low_ids[:, None] == target[None, :], interp_band[:, column][None, :], jnp.float32(0.0)
        )
    return dense.astype(jnp.bfloat16)


def shift_up(values, cosines, sines):
    real_part = values[:, :, 0, :] * cosines - values[:, :, 1, :] * sines
    imag_part = values[:, :, 0, :] * sines + values[:, :, 1, :] * cosines
    return jnp.stack([real_part, imag_part], axis=2)


def shift_down(values, cosines, sines):
    real_in = values[:, None, 0, :]
    imag_in = values[:, None, 1, :]
    real_part = real_in * cosines + imag_in * sines
    imag_part = imag_in * cosines - real_in * sines
    return jnp.stack([real_part, imag_part], axis=2)


def translate(window, translation, rel_box, classes, counts):
    rows, far = classes.shape
    width = window.shape[0]
    nclass = translation.shape[0]
    slots = jnp.arange(far, dtype=jnp.int32)
    live = slots[None, :] < counts[:, None]
    box_t = rel_box.T.reshape(-1)
    cls_t = classes.T.reshape(-1)
    live_t = live.T.reshape(-1)
    pick_box = jnp.logical_and(
        box_t[:, None] == jnp.arange(width, dtype=jnp.int32)[None, :], live_t[:, None]
    ).astype(jnp.bfloat16)
    pick_cls = (cls_t[:, None] == jnp.arange(nclass, dtype=jnp.int32)[None, :]).astype(jnp.bfloat16)
    pick_cls = jnp.concatenate([pick_cls, pick_cls], axis=1)
    high = translation.astype(jnp.bfloat16)
    low = (translation - high.astype(jnp.float32)).astype(jnp.bfloat16)
    op_re = jnp.concatenate([high[:, 0], low[:, 0]], axis=0)
    op_im = jnp.concatenate([high[:, 1], low[:, 1]], axis=0)
    f32 = jnp.float32
    t_re = jnp.dot(pick_cls, op_re, preferred_element_type=f32)
    t_im = jnp.dot(pick_cls, op_im, preferred_element_type=f32)
    p_re = jnp.dot(pick_box, window[:, 0], preferred_element_type=f32)
    p_im = jnp.dot(pick_box, window[:, 1], preferred_element_type=f32)
    real_part = (t_re * p_re - t_im * p_im).reshape(far, rows, -1).sum(axis=0)
    imag_part = (t_re * p_im + t_im * p_re).reshape(far, rows, -1).sum(axis=0)
    return jnp.stack([real_part, imag_part], axis=1)


def make_body(box_count, ang_count):
    devices = box_count * ang_count

    def body(
        children, interp_band, band_start, shift_angle, far_box, far_class, far_count, translation
    ):
        high_width = interp_band.shape[0]
        low_width = children.shape[2]
        parents_here = children.shape[0] // 8
        assert parents_here >= REACH
        interp = build_interp(interp_band, band_start)
        raised = jnp.dot(children.reshape(-1, low_width), interp, preferred_element_type=jnp.float32)
        raised = raised.reshape(-1, 8, 2, high_width)
        cosines = jnp.cos(shift_angle)
        sines = jnp.sin(shift_angle)
        parent = jnp.sum(shift_up(raised, cosines, sines), axis=1).astype(jnp.bfloat16)
        axes = ("box", "ang")
        up = [(i, i + 1) for i in range(devices - 1)]
        down = [(i + 1, i) for i in range(devices - 1)]
        before = lax.ppermute(parent[parents_here - REACH:], axes, up)
        after = lax.ppermute(parent[:REACH], axes, down)
        window = jnp.concatenate([before, parent, after], axis=0)
        ang = lax.axis_index("ang")
        device = lax.axis_index("box") * ang_count + ang
        first = ang * parents_here
        my_box = lax.dynamic_slice_in_dim(far_box, first, parents_here, 0)
        my_class = lax.dynamic_slice_in_dim(far_class, first, parents_here, 0)
        my_count = lax.dynamic_slice_in_dim(far_count, first, parents_here, 0)
        rel_box = my_box - (device * parents_here - REACH)
        local = translate(window, translation, rel_box, my_class, my_count).astype(jnp.bfloat16)
        spread = shift_down(local.astype(jnp.float32), cosines, sines).astype(jnp.bfloat16)
        result = jnp.dot(spread.reshape(-1, high_width), interp.T, preferred_element_type=jnp.float32)
        return result.reshape(-1, 2, low_width)

    return body


def solution(mesh):
    return jax.shard_map(
        make_body(mesh.shape["box"], mesh.shape["ang"]),
        mesh=mesh,
        in_specs=(
            P(("box", "ang"), None, None),
            P(),
            P(),
            P(),
            P("box", None),
            P("box", None),
            P("box"),
            P(),
        ),
        out_specs=P(("box", "ang"), None, None),
        check_vma=False,
    )
```

```python
import jax
import jax.numpy as jnp
from jax import lax
from jax.sharding import PartitionSpec as P

K_LOW = 1024
REACH = 16


def build_interp(interp_band, band_start):
    low_ids = jnp.arange(K_LOW, dtype=jnp.int32)
    dense = jnp.zeros((K_LOW, interp_band.shape[0]), jnp.float32)
    for column in range(interp_band.shape[1]):
        target = band_start + column
        dense = dense + jnp.where(
            low_ids[:, None] == target[None, :], interp_band[:, column][None, :], jnp.float32(0.0)
        )
    return dense.astype(jnp.bfloat16)


def translate(window, translation, rel_box, classes, counts):
    rows, far = classes.shape
    width = window.shape[1]
    nclass = translation.shape[0]
    slots = jnp.arange(far, dtype=jnp.int32)
    live = slots[None, :] < counts[:, None]
    box_t = rel_box.T.reshape(-1)
    cls_t = classes.T.reshape(-1)
    live_t = live.T.reshape(-1)
    pick_box = jnp.logical_and(
        box_t[:, None] == jnp.arange(width, dtype=jnp.int32)[None, :], live_t[:, None]
    ).astype(jnp.bfloat16)
    pick_cls = (cls_t[:, None] == jnp.arange(nclass, dtype=jnp.int32)[None, :]).astype(jnp.bfloat16)
    pick_cls = jnp.concatenate([pick_cls, pick_cls], axis=1)
    op_re = split_parts(translation[:, 0])
    op_im = split_parts(translation[:, 1])
    f32 = jnp.float32
    t_re = jnp.dot(pick_cls, op_re, preferred_element_type=f32)
    t_im = jnp.dot(pick_cls, op_im, preferred_element_type=f32)
    p_re = jnp.dot(pick_box, window[0], preferred_element_type=f32)
    p_im = jnp.dot(pick_box, window[1], preferred_element_type=f32)
    real_part = (t_re * p_re - t_im * p_im).reshape(far, rows, -1).sum(axis=0)
    imag_part = (t_re * p_im + t_im * p_re).reshape(far, rows, -1).sum(axis=0)
    return real_part, imag_part


def split_parts(values):
    high = values.astype(jnp.bfloat16)
    low = (values - high.astype(jnp.float32)).astype(jnp.bfloat16)
    return jnp.concatenate([high, low], axis=0)


def make_body(box_count, ang_count):
    devices = box_count * ang_count

    def body(
        children, interp_band, band_start, shift_angle, far_box, far_class, far_count, translation
    ):
        high_width = interp_band.shape[0]
        low_width = children.shape[2]
        parents_here = children.shape[0] // 8
        assert parents_here >= REACH
        f32 = jnp.float32
        interp = lax.optimization_barrier(build_interp(interp_band, band_start))
        raised_re = jnp.dot(children[:, 0], interp, preferred_element_type=f32).reshape(-1, 8, high_width)
        raised_im = jnp.dot(children[:, 1], interp, preferred_element_type=f32).reshape(-1, 8, high_width)
        cosines = jnp.cos(shift_angle)
        sines = jnp.sin(shift_angle)
        parent_re = jnp.sum(raised_re * cosines - raised_im * sines, axis=1)
        parent_im = jnp.sum(raised_re * sines + raised_im * cosines, axis=1)
        parent = jnp.stack([parent_re, parent_im]).astype(jnp.bfloat16)
        axes = ("box", "ang")
        up = [(i, i + 1) for i in range(devices - 1)]
        down = [(i + 1, i) for i in range(devices - 1)]
        before = lax.ppermute(parent[:, parents_here - REACH:], axes, up)
        after = lax.ppermute(parent[:, :REACH], axes, down)
        window = jnp.concatenate([before, parent, after], axis=1)
        ang = lax.axis_index("ang")
        device = lax.axis_index("box") * ang_count + ang
        first = ang * parents_here
        my_box = lax.dynamic_slice_in_dim(far_box, first, parents_here, 0)
        my_class = lax.dynamic_slice_in_dim(far_class, first, parents_here, 0)
        my_count = lax.dynamic_slice_in_dim(far_count, first, parents_here, 0)
        rel_box = my_box - (device * parents_here - REACH)
        local_re, local_im = translate(window, translation, rel_box, my_class, my_count)
        local_re = lax.reduce_precision(local_re, exponent_bits=8, mantissa_bits=7)[:, None]
        local_im = lax.reduce_precision(local_im, exponent_bits=8, mantissa_bits=7)[:, None]
        spread_re = (local_re * cosines + local_im * sines).astype(jnp.bfloat16).reshape(-1, high_width)
        spread_im = (local_im * cosines - local_re * sines).astype(jnp.bfloat16).reshape(-1, high_width)
        contract = (((1,), (1,)), ((), ()))
        out_re = lax.dot_general(spread_re, interp, contract, preferred_element_type=f32)
        out_im = lax.dot_general(spread_im, interp, contract, preferred_element_type=f32)
        return jnp.stack([out_re, out_im], axis=1)

    return body


def solution(mesh):
    return jax.shard_map(
        make_body(mesh.shape["box"], mesh.shape["ang"]),
        mesh=mesh,
        in_specs=(
            P(("box", "ang"), None, None),
            P(),
            P(),
            P(),
            P("box", None),
            P("box", None),
            P("box"),
            P(),
        ),
        out_specs=P(("box", "ang"), None, None),
        check_vma=False,
    )
```

```python
import jax
import jax.numpy as jnp
from jax import lax
from jax.sharding import PartitionSpec as P

K_LOW = 1024
REACH = 16


def build_interp(interp_band, band_start):
    low_ids = jnp.arange(K_LOW, dtype=jnp.int32)
    dense = jnp.zeros((K_LOW, interp_band.shape[0]), jnp.float32)
    for column in range(interp_band.shape[1]):
        target = band_start + column
        dense = dense + jnp.where(
            low_ids[:, None] == target[None, :], interp_band[:, column][None, :], jnp.float32(0.0)
        )
    return dense.astype(jnp.bfloat16)


def translate(window, translation, rel_box, classes, counts):
    rows, far = classes.shape
    width = window.shape[1]
    nclass = translation.shape[0]
    slots = jnp.arange(far, dtype=jnp.int32)
    live = slots[None, :] < counts[:, None]
    box_t = rel_box.T.reshape(-1)
    cls_t = classes.T.reshape(-1)
    live_t = live.T.reshape(-1)
    pick_box = jnp.logical_and(
        box_t[:, None] == jnp.arange(width, dtype=jnp.int32)[None, :], live_t[:, None]
    ).astype(jnp.bfloat16)
    pick_cls = (cls_t[:, None] == jnp.arange(nclass, dtype=jnp.int32)[None, :]).astype(jnp.bfloat16)
    pick_cls = jnp.concatenate([pick_cls, pick_cls], axis=1)
    f32 = jnp.float32
    picked = lax.dot_general(
        pick_cls, split_parts(translation), (((1,), (0,)), ((), ())), preferred_element_type=f32
    )
    t_re = picked[:, 0]
    t_im = picked[:, 1]
    p_re = jnp.dot(pick_box, window[0], preferred_element_type=f32)
    p_im = jnp.dot(pick_box, window[1], preferred_element_type=f32)
    real_part = (t_re * p_re - t_im * p_im).reshape(far, rows, -1).sum(axis=0)
    imag_part = (t_re * p_im + t_im * p_re).reshape(far, rows, -1).sum(axis=0)
    return real_part, imag_part


def split_parts(values):
    high = lax.reduce_precision(values, exponent_bits=8, mantissa_bits=7)
    low = values - high
    return jnp.concatenate([high.astype(jnp.bfloat16), low.astype(jnp.bfloat16)], axis=0)


def make_body(box_count, ang_count):
    devices = box_count * ang_count

    def body(
        children, interp_band, band_start, shift_angle, far_box, far_class, far_count, translation
    ):
        high_width = interp_band.shape[0]
        low_width = children.shape[2]
        parents_here = children.shape[0] // 8
        assert parents_here >= REACH
        f32 = jnp.float32
        interp = lax.optimization_barrier(build_interp(interp_band, band_start))
        raised_re = jnp.dot(children[:, 0], interp, preferred_element_type=f32).reshape(-1, 8, high_width)
        raised_im = jnp.dot(children[:, 1], interp, preferred_element_type=f32).reshape(-1, 8, high_width)
        cosines = jnp.cos(shift_angle)
        sines = jnp.sin(shift_angle)
        parent_re = jnp.sum(raised_re * cosines - raised_im * sines, axis=1)
        parent_im = jnp.sum(raised_re * sines + raised_im * cosines, axis=1)
        parent = jnp.stack([parent_re, parent_im]).astype(jnp.bfloat16)
        axes = ("box", "ang")
        up = [(i, i + 1) for i in range(devices - 1)]
        down = [(i + 1, i) for i in range(devices - 1)]
        before = lax.ppermute(parent[:, parents_here - REACH:], axes, up)
        after = lax.ppermute(parent[:, :REACH], axes, down)
        window = jnp.concatenate([before, parent, after], axis=1)
        ang = lax.axis_index("ang")
        device = lax.axis_index("box") * ang_count + ang
        first = ang * parents_here
        my_box = lax.dynamic_slice_in_dim(far_box, first, parents_here, 0)
        my_class = lax.dynamic_slice_in_dim(far_class, first, parents_here, 0)
        my_count = lax.dynamic_slice_in_dim(far_count, first, parents_here, 0)
        rel_box = my_box - (device * parents_here - REACH)
        local_re, local_im = translate(window, translation, rel_box, my_class, my_count)
        local_re = lax.reduce_precision(local_re, exponent_bits=8, mantissa_bits=7)[:, None]
        local_im = lax.reduce_precision(local_im, exponent_bits=8, mantissa_bits=7)[:, None]
        spread_re = (local_re * cosines + local_im * sines).astype(jnp.bfloat16).reshape(-1, high_width)
        spread_im = (local_im * cosines - local_re * sines).astype(jnp.bfloat16).reshape(-1, high_width)
        contract = (((1,), (1,)), ((), ()))
        out_re = lax.dot_general(spread_re, interp, contract, preferred_element_type=f32)
        out_im = lax.dot_general(spread_im, interp, contract, preferred_element_type=f32)
        return jnp.stack([out_re, out_im], axis=1)

    return body


def solution(mesh):
    return jax.shard_map(
        make_body(mesh.shape["box"], mesh.shape["ang"]),
        mesh=mesh,
        in_specs=(
            P(("box", "ang"), None, None),
            P(),
            P(),
            P(),
            P("box", None),
            P("box", None),
            P("box"),
            P(),
        ),
        out_specs=P(("box", "ang"), None, None),
        check_vma=False,
    )
```

```python
import jax
import jax.numpy as jnp
from jax import lax
from jax.sharding import PartitionSpec as P
from jax.experimental import pallas as pl

INTERPRET = False
CHUNK = 512

K_LOW = 1024
REACH = 16


def build_interp(interp_band, band_start):
    offset = jnp.arange(K_LOW, dtype=jnp.int32)[:, None] - band_start[None, :]
    weights = interp_band.T
    dense = jnp.zeros((K_LOW, interp_band.shape[0]), jnp.float32)
    for column in range(interp_band.shape[1]):
        dense = jnp.where(offset == column, weights[column][None, :], dense)
    return dense.astype(jnp.bfloat16)


def translate_kernel(pick_cls_ref, pick_box_ref, ops_ref, win_ref, out_ref):
    f32 = jnp.float32
    pick_cls = pick_cls_ref[...]
    pick_box = pick_box_ref[...]
    t_re = jnp.dot(pick_cls, ops_ref[0], preferred_element_type=f32)
    t_im = jnp.dot(pick_cls, ops_ref[1], preferred_element_type=f32)
    p_re = jnp.dot(pick_box, win_ref[0], preferred_element_type=f32)
    p_im = jnp.dot(pick_box, win_ref[1], preferred_element_type=f32)
    real_part = t_re * p_re - t_im * p_im
    imag_part = t_re * p_im + t_im * p_re
    rows = out_ref.shape[1]
    acc_re = real_part[0:rows]
    acc_im = imag_part[0:rows]
    for slot in range(1, real_part.shape[0] // rows):
        acc_re = acc_re + real_part[slot * rows:(slot + 1) * rows]
        acc_im = acc_im + imag_part[slot * rows:(slot + 1) * rows]
    out_ref[0] = acc_re.astype(out_ref.dtype)
    out_ref[1] = acc_im.astype(out_ref.dtype)


def translate(window, translation, rel_box, classes, counts):
    rows, far = classes.shape
    width = window.shape[1]
    nclass = translation.shape[0]
    slots = jnp.arange(far, dtype=jnp.int32)
    live = slots[None, :] < counts[:, None]
    box_t = rel_box.T.reshape(-1)
    cls_t = classes.T.reshape(-1)
    live_t = live.T.reshape(-1)
    pick_box = jnp.logical_and(
        box_t[:, None] == jnp.arange(width, dtype=jnp.int32)[None, :], live_t[:, None]
    ).astype(jnp.bfloat16)
    pick_cls = (cls_t[:, None] == jnp.arange(nclass, dtype=jnp.int32)[None, :]).astype(jnp.bfloat16)
    pick_cls = jnp.concatenate([pick_cls, pick_cls], axis=1)
    ops = split_parts(translation).transpose(1, 0, 2)
    k_high = window.shape[2]
    slots_rows = pick_cls.shape[0]
    return pl.pallas_call(
        translate_kernel,
        out_shape=jax.ShapeDtypeStruct((2, rows, k_high), jnp.bfloat16),
        grid=(k_high // CHUNK,),
        in_specs=[
            pl.BlockSpec((slots_rows, pick_cls.shape[1]), lambda j: (0, 0)),
            pl.BlockSpec((slots_rows, width), lambda j: (0, 0)),
            pl.BlockSpec((2, ops.shape[1], CHUNK), lambda j: (0, 0, j)),
            pl.BlockSpec((2, width, CHUNK), lambda j: (0, 0, j)),
        ],
        out_specs=pl.BlockSpec((2, rows, CHUNK), lambda j: (0, 0, j)),
        interpret=INTERPRET,
    )(pick_cls, pick_box, ops, window)


def split_parts(values):
    high = lax.reduce_precision(values, exponent_bits=8, mantissa_bits=7)
    low = values - high
    return jnp.concatenate([high.astype(jnp.bfloat16), low.astype(jnp.bfloat16)], axis=0)


def make_body(box_count, ang_count):
    devices = box_count * ang_count

    def body(
        children, interp_band, band_start, shift_angle, far_box, far_class, far_count, translation
    ):
        high_width = interp_band.shape[0]
        low_width = children.shape[2]
        parents_here = children.shape[0] // 8
        assert parents_here >= REACH
        f32 = jnp.float32
        interp = lax.optimization_barrier(build_interp(interp_band, band_start))
        raised_re = jnp.dot(children[:, 0], interp, preferred_element_type=f32).reshape(-1, 8, high_width)
        raised_im = jnp.dot(children[:, 1], interp, preferred_element_type=f32).reshape(-1, 8, high_width)
        cosines = jnp.cos(shift_angle)
        sines = jnp.sin(shift_angle)
        parent_re = jnp.sum(raised_re * cosines - raised_im * sines, axis=1)
        parent_im = jnp.sum(raised_re * sines + raised_im * cosines, axis=1)
        parent = jnp.stack([parent_re, parent_im]).astype(jnp.bfloat16)
        axes = ("box", "ang")
        up = [(i, i + 1) for i in range(devices - 1)]
        down = [(i + 1, i) for i in range(devices - 1)]
        before = lax.ppermute(parent[:, parents_here - REACH:], axes, up)
        after = lax.ppermute(parent[:, :REACH], axes, down)
        window = jnp.concatenate([before, parent, after], axis=1)
        ang = lax.axis_index("ang")
        device = lax.axis_index("box") * ang_count + ang
        first = ang * parents_here
        my_box = lax.dynamic_slice_in_dim(far_box, first, parents_here, 0)
        my_class = lax.dynamic_slice_in_dim(far_class, first, parents_here, 0)
        my_count = lax.dynamic_slice_in_dim(far_count, first, parents_here, 0)
        rel_box = my_box - (device * parents_here - REACH)
        local = translate(window, translation, rel_box, my_class, my_count).astype(f32)
        local_re = local[0][:, None]
        local_im = local[1][:, None]
        spread_re = (local_re * cosines + local_im * sines).astype(jnp.bfloat16).reshape(-1, high_width)
        spread_im = (local_im * cosines - local_re * sines).astype(jnp.bfloat16).reshape(-1, high_width)
        contract = (((1,), (1,)), ((), ()))
        out_re = lax.dot_general(spread_re, interp, contract, preferred_element_type=f32)
        out_im = lax.dot_general(spread_im, interp, contract, preferred_element_type=f32)
        return jnp.stack([out_re, out_im], axis=1)

    return body


def solution(mesh):
    return jax.shard_map(
        make_body(mesh.shape["box"], mesh.shape["ang"]),
        mesh=mesh,
        in_specs=(
            P(("box", "ang"), None, None),
            P(),
            P(),
            P(),
            P("box", None),
            P("box", None),
            P("box"),
            P(),
        ),
        out_specs=P(("box", "ang"), None, None),
        check_vma=False,
    )
```

```python
import jax
import jax.numpy as jnp
from jax import lax
from jax.sharding import PartitionSpec as P
from jax.experimental import pallas as pl

INTERPRET = False
CHUNK = 512

K_LOW = 1024
REACH = 16


def build_interp(interp_band, band_start):
    offset = jnp.arange(K_LOW, dtype=jnp.int32)[:, None] - band_start[None, :]
    weights = interp_band.T
    dense = jnp.zeros((K_LOW, interp_band.shape[0]), jnp.float32)
    for column in range(interp_band.shape[1]):
        dense = jnp.where(offset == column, weights[column][None, :], dense)
    return dense.astype(jnp.bfloat16)


def translate_kernel(pick_cls_ref, pick_box_ref, high_ref, low_ref, win_ref, out_ref):
    f32 = jnp.float32
    pick_cls = pick_cls_ref[...]
    pick_box = pick_box_ref[...]
    t_re = jnp.dot(pick_cls, high_ref[0], preferred_element_type=f32)
    t_re = t_re + jnp.dot(pick_cls, low_ref[0], preferred_element_type=f32)
    t_im = jnp.dot(pick_cls, high_ref[1], preferred_element_type=f32)
    t_im = t_im + jnp.dot(pick_cls, low_ref[1], preferred_element_type=f32)
    p_re = jnp.dot(pick_box, win_ref[0], preferred_element_type=f32)
    p_im = jnp.dot(pick_box, win_ref[1], preferred_element_type=f32)
    real_part = t_re * p_re - t_im * p_im
    imag_part = t_re * p_im + t_im * p_re
    rows = out_ref.shape[1]
    acc_re = real_part[0:rows]
    acc_im = imag_part[0:rows]
    for slot in range(1, real_part.shape[0] // rows):
        acc_re = acc_re + real_part[slot * rows:(slot + 1) * rows]
        acc_im = acc_im + imag_part[slot * rows:(slot + 1) * rows]
    out_ref[0] = acc_re.astype(out_ref.dtype)
    out_ref[1] = acc_im.astype(out_ref.dtype)


def translate(window, translation, rel_box, classes, counts):
    rows, far = classes.shape
    width = window.shape[1]
    nclass = translation.shape[0]
    slots = jnp.arange(far, dtype=jnp.int32)
    live = slots[None, :] < counts[:, None]
    box_t = rel_box.T.reshape(-1)
    cls_t = classes.T.reshape(-1)
    live_t = live.T.reshape(-1)
    pick_box = jnp.logical_and(
        box_t[:, None] == jnp.arange(width, dtype=jnp.int32)[None, :], live_t[:, None]
    ).astype(jnp.bfloat16)
    pick_cls = (cls_t[:, None] == jnp.arange(nclass, dtype=jnp.int32)[None, :]).astype(jnp.bfloat16)
    high, low = split_parts(translation.transpose(1, 0, 2))
    k_high = window.shape[2]
    slots_rows = pick_cls.shape[0]
    return pl.pallas_call(
        translate_kernel,
        out_shape=jax.ShapeDtypeStruct((2, rows, k_high), jnp.bfloat16),
        grid=(k_high // CHUNK,),
        in_specs=[
            pl.BlockSpec((slots_rows, pick_cls.shape[1]), lambda j: (0, 0)),
            pl.BlockSpec((slots_rows, width), lambda j: (0, 0)),
            pl.BlockSpec((2, nclass, CHUNK), lambda j: (0, 0, j)),
            pl.BlockSpec((2, nclass, CHUNK), lambda j: (0, 0, j)),
            pl.BlockSpec((2, width, CHUNK), lambda j: (0, 0, j)),
        ],
        out_specs=pl.BlockSpec((2, rows, CHUNK), lambda j: (0, 0, j)),
        interpret=INTERPRET,
    )(pick_cls, pick_box, high, low, window)


def split_parts(values):
    high = lax.reduce_precision(values, exponent_bits=8, mantissa_bits=7)
    low = values - high
    return high.astype(jnp.bfloat16), low.astype(jnp.bfloat16)


def make_body(box_count, ang_count):
    devices = box_count * ang_count

    def body(
        children, interp_band, band_start, shift_angle, far_box, far_class, far_count, translation
    ):
        high_width = interp_band.shape[0]
        low_width = children.shape[2]
        parents_here = children.shape[0] // 8
        assert parents_here >= REACH
        f32 = jnp.float32
        interp = lax.optimization_barrier(build_interp(interp_band, band_start))
        raised_re = jnp.dot(children[:, 0], interp, preferred_element_type=f32).reshape(-1, 8, high_width)
        raised_im = jnp.dot(children[:, 1], interp, preferred_element_type=f32).reshape(-1, 8, high_width)
        cosines = jnp.cos(shift_angle)
        sines = jnp.sin(shift_angle)
        parent_re = jnp.sum(raised_re * cosines - raised_im * sines, axis=1)
        parent_im = jnp.sum(raised_re * sines + raised_im * cosines, axis=1)
        parent = jnp.stack([parent_re, parent_im]).astype(jnp.bfloat16)
        axes = ("box", "ang")
        up = [(i, i + 1) for i in range(devices - 1)]
        down = [(i + 1, i) for i in range(devices - 1)]
        before = lax.ppermute(parent[:, parents_here - REACH:], axes, up)
        after = lax.ppermute(parent[:, :REACH], axes, down)
        window = jnp.concatenate([before, parent, after], axis=1)
        ang = lax.axis_index("ang")
        device = lax.axis_index("box") * ang_count + ang
        first = ang * parents_here
        my_box = lax.dynamic_slice_in_dim(far_box, first, parents_here, 0)
        my_class = lax.dynamic_slice_in_dim(far_class, first, parents_here, 0)
        my_count = lax.dynamic_slice_in_dim(far_count, first, parents_here, 0)
        rel_box = my_box - (device * parents_here - REACH)
        local = translate(window, translation, rel_box, my_class, my_count).astype(f32)
        local_re = local[0][:, None]
        local_im = local[1][:, None]
        spread_re = (local_re * cosines + local_im * sines).astype(jnp.bfloat16).reshape(-1, high_width)
        spread_im = (local_im * cosines - local_re * sines).astype(jnp.bfloat16).reshape(-1, high_width)
        contract = (((1,), (1,)), ((), ()))
        out_re = lax.dot_general(spread_re, interp, contract, preferred_element_type=f32)
        out_im = lax.dot_general(spread_im, interp, contract, preferred_element_type=f32)
        return jnp.stack([out_re, out_im], axis=1)

    return body


def solution(mesh):
    return jax.shard_map(
        make_body(mesh.shape["box"], mesh.shape["ang"]),
        mesh=mesh,
        in_specs=(
            P(("box", "ang"), None, None),
            P(),
            P(),
            P(),
            P("box", None),
            P("box", None),
            P("box"),
            P(),
        ),
        out_specs=P(("box", "ang"), None, None),
        check_vma=False,
    )
```

```python
import jax
import jax.numpy as jnp
from jax import lax
from jax.sharding import PartitionSpec as P
from jax.experimental import pallas as pl

INTERPRET = False
CHUNK = 512

K_LOW = 1024
REACH = 16


def build_interp(interp_band, band_start):
    offset = jnp.arange(K_LOW, dtype=jnp.int32)[:, None] - band_start[None, :]
    weights = interp_band.T
    dense = jnp.zeros((K_LOW, interp_band.shape[0]), jnp.float32)
    for column in range(interp_band.shape[1]):
        dense = jnp.where(offset == column, weights[column][None, :], dense)
    return dense.astype(jnp.bfloat16)


def translate_kernel(pick_cls_ref, pick_box_ref, ops_ref, win_ref, cos_ref, sin_ref, out_ref):
    f32 = jnp.float32
    pick_cls = pick_cls_ref[...]
    pick_box = pick_box_ref[...]
    t_re = jnp.dot(pick_cls, ops_ref[0], preferred_element_type=f32)
    t_im = jnp.dot(pick_cls, ops_ref[1], preferred_element_type=f32)
    p_re = jnp.dot(pick_box, win_ref[0], preferred_element_type=f32)
    p_im = jnp.dot(pick_box, win_ref[1], preferred_element_type=f32)
    real_part = t_re * p_re - t_im * p_im
    imag_part = t_re * p_im + t_im * p_re
    rows = out_ref.shape[1] // 8
    acc_re = real_part[0:rows]
    acc_im = imag_part[0:rows]
    for slot in range(1, real_part.shape[0] // rows):
        acc_re = acc_re + real_part[slot * rows:(slot + 1) * rows]
        acc_im = acc_im + imag_part[slot * rows:(slot + 1) * rows]
    local_re = acc_re.astype(jnp.bfloat16).astype(f32)[:, None, :]
    local_im = acc_im.astype(jnp.bfloat16).astype(f32)[:, None, :]
    cosines = cos_ref[...][None]
    sines = sin_ref[...][None]
    spread_re = local_re * cosines + local_im * sines
    spread_im = local_im * cosines - local_re * sines
    out_ref[0] = spread_re.reshape(out_ref.shape[1], -1).astype(out_ref.dtype)
    out_ref[1] = spread_im.reshape(out_ref.shape[1], -1).astype(out_ref.dtype)


def translate(window, translation, rel_box, classes, counts, cosines, sines):
    rows, far = classes.shape
    width = window.shape[1]
    nclass = translation.shape[0]
    slots = jnp.arange(far, dtype=jnp.int32)
    live = slots[None, :] < counts[:, None]
    box_t = rel_box.T.reshape(-1)
    cls_t = classes.T.reshape(-1)
    live_t = live.T.reshape(-1)
    pick_box = jnp.logical_and(
        box_t[:, None] == jnp.arange(width, dtype=jnp.int32)[None, :], live_t[:, None]
    ).astype(jnp.bfloat16)
    pick_cls = (cls_t[:, None] == jnp.arange(nclass, dtype=jnp.int32)[None, :]).astype(jnp.bfloat16)
    pick_cls = jnp.concatenate([pick_cls, pick_cls], axis=1)
    ops = split_parts(translation).transpose(1, 0, 2)
    k_high = window.shape[2]
    slots_rows = pick_cls.shape[0]
    return pl.pallas_call(
        translate_kernel,
        out_shape=jax.ShapeDtypeStruct((2, rows * 8, k_high), jnp.bfloat16),
        grid=(k_high // CHUNK,),
        in_specs=[
            pl.BlockSpec((slots_rows, pick_cls.shape[1]), lambda j: (0, 0)),
            pl.BlockSpec((slots_rows, width), lambda j: (0, 0)),
            pl.BlockSpec((2, ops.shape[1], CHUNK), lambda j: (0, 0, j)),
            pl.BlockSpec((2, width, CHUNK), lambda j: (0, 0, j)),
            pl.BlockSpec((8, CHUNK), lambda j: (0, j)),
            pl.BlockSpec((8, CHUNK), lambda j: (0, j)),
        ],
        out_specs=pl.BlockSpec((2, rows * 8, CHUNK), lambda j: (0, 0, j)),
        interpret=INTERPRET,
    )(pick_cls, pick_box, ops, window, cosines, sines)


def split_parts(values):
    high = lax.reduce_precision(values, exponent_bits=8, mantissa_bits=7)
    low = values - high
    return jnp.concatenate([high.astype(jnp.bfloat16), low.astype(jnp.bfloat16)], axis=0)


def make_body(box_count, ang_count):
    devices = box_count * ang_count

    def body(
        children, interp_band, band_start, shift_angle, far_box, far_class, far_count, translation
    ):
        high_width = interp_band.shape[0]
        low_width = children.shape[2]
        parents_here = children.shape[0] // 8
        assert parents_here >= REACH
        f32 = jnp.float32
        interp = lax.optimization_barrier(build_interp(interp_band, band_start))
        raised_re = jnp.dot(children[:, 0], interp, preferred_element_type=f32).reshape(-1, 8, high_width)
        raised_im = jnp.dot(children[:, 1], interp, preferred_element_type=f32).reshape(-1, 8, high_width)
        cosines = jnp.cos(shift_angle)
        sines = jnp.sin(shift_angle)
        parent_re = jnp.sum(raised_re * cosines - raised_im * sines, axis=1)
        parent_im = jnp.sum(raised_re * sines + raised_im * cosines, axis=1)
        parent = jnp.stack([parent_re, parent_im]).astype(jnp.bfloat16)
        axes = ("box", "ang")
        up = [(i, i + 1) for i in range(devices - 1)]
        down = [(i + 1, i) for i in range(devices - 1)]
        before = lax.ppermute(parent[:, parents_here - REACH:], axes, up)
        after = lax.ppermute(parent[:, :REACH], axes, down)
        window = jnp.concatenate([before, parent, after], axis=1)
        ang = lax.axis_index("ang")
        device = lax.axis_index("box") * ang_count + ang
        first = ang * parents_here
        my_box = lax.dynamic_slice_in_dim(far_box, first, parents_here, 0)
        my_class = lax.dynamic_slice_in_dim(far_class, first, parents_here, 0)
        my_count = lax.dynamic_slice_in_dim(far_count, first, parents_here, 0)
        rel_box = my_box - (device * parents_here - REACH)
        spread = translate(window, translation, rel_box, my_class, my_count, cosines, sines)
        spread_re = spread[0]
        spread_im = spread[1]
        contract = (((1,), (1,)), ((), ()))
        out_re = lax.dot_general(spread_re, interp, contract, preferred_element_type=f32)
        out_im = lax.dot_general(spread_im, interp, contract, preferred_element_type=f32)
        return jnp.stack([out_re, out_im], axis=1)

    return body


def solution(mesh):
    return jax.shard_map(
        make_body(mesh.shape["box"], mesh.shape["ang"]),
        mesh=mesh,
        in_specs=(
            P(("box", "ang"), None, None),
            P(),
            P(),
            P(),
            P("box", None),
            P("box", None),
            P("box"),
            P(),
        ),
        out_specs=P(("box", "ang"), None, None),
        check_vma=False,
    )
```

```python
import jax
import jax.numpy as jnp
from jax import lax
from jax.sharding import PartitionSpec as P
from jax.experimental import pallas as pl

INTERPRET = False
CHUNK = 512

K_LOW = 1024
REACH = 16


def build_interp(interp_band, band_start):
    offset = jnp.arange(K_LOW, dtype=jnp.int32)[:, None] - band_start[None, :]
    weights = interp_band.T
    dense = jnp.zeros((K_LOW, interp_band.shape[0]), jnp.float32)
    for column in range(interp_band.shape[1]):
        dense = jnp.where(offset == column, weights[column][None, :], dense)
    return dense.astype(jnp.bfloat16)


def translate_kernel(pick_cls_ref, pick_box_ref, ops_ref, win_ref, cos_ref, sin_ref, out_ref):
    f32 = jnp.float32
    pick_cls = pick_cls_ref[...]
    pick_box = pick_box_ref[...]
    t_re = jnp.dot(pick_cls, ops_ref[0], preferred_element_type=f32)
    t_im = jnp.dot(pick_cls, ops_ref[1], preferred_element_type=f32)
    p_re = jnp.dot(pick_box, win_ref[0], preferred_element_type=f32)
    p_im = jnp.dot(pick_box, win_ref[1], preferred_element_type=f32)
    real_part = t_re * p_re - t_im * p_im
    imag_part = t_re * p_im + t_im * p_re
    rows = out_ref.shape[1] // 8
    acc_re = real_part[0:rows]
    acc_im = imag_part[0:rows]
    for slot in range(1, real_part.shape[0] // rows):
        acc_re = acc_re + real_part[slot * rows:(slot + 1) * rows]
        acc_im = acc_im + imag_part[slot * rows:(slot + 1) * rows]
    local_re = acc_re.astype(jnp.bfloat16).astype(f32)[:, None, :]
    local_im = acc_im.astype(jnp.bfloat16).astype(f32)[:, None, :]
    cosines = cos_ref[...][None]
    sines = sin_ref[...][None]
    spread_re = local_re * cosines + local_im * sines
    spread_im = local_im * cosines - local_re * sines
    out_ref[0] = spread_re.reshape(out_ref.shape[1], -1).astype(out_ref.dtype)
    out_ref[1] = spread_im.reshape(out_ref.shape[1], -1).astype(out_ref.dtype)


def translate(window, translation, rel_box, classes, counts, cosines, sines):
    rows, far = classes.shape
    width = window.shape[1]
    nclass = translation.shape[0]
    slots = jnp.arange(far, dtype=jnp.int32)
    live = slots[None, :] < counts[:, None]
    box_t = rel_box.T.reshape(-1)
    cls_t = classes.T.reshape(-1)
    live_t = live.T.reshape(-1)
    pick_box = jnp.logical_and(
        box_t[:, None] == jnp.arange(width, dtype=jnp.int32)[None, :], live_t[:, None]
    ).astype(jnp.bfloat16)
    pick_cls = (cls_t[:, None] == jnp.arange(nclass, dtype=jnp.int32)[None, :]).astype(jnp.bfloat16)
    pick_cls = jnp.concatenate([pick_cls, pick_cls], axis=1)
    ops = split_parts(translation).transpose(1, 0, 2)
    k_high = window.shape[2]
    slots_rows = pick_cls.shape[0]
    return pl.pallas_call(
        translate_kernel,
        out_shape=jax.ShapeDtypeStruct((2, rows * 8, k_high), jnp.bfloat16),
        grid=(k_high // CHUNK,),
        in_specs=[
            pl.BlockSpec((slots_rows, pick_cls.shape[1]), lambda j: (0, 0)),
            pl.BlockSpec((slots_rows, width), lambda j: (0, 0)),
            pl.BlockSpec((2, ops.shape[1], CHUNK), lambda j: (0, 0, j)),
            pl.BlockSpec((2, width, CHUNK), lambda j: (0, 0, j)),
            pl.BlockSpec((8, CHUNK), lambda j: (0, j)),
            pl.BlockSpec((8, CHUNK), lambda j: (0, j)),
        ],
        out_specs=pl.BlockSpec((2, rows * 8, CHUNK), lambda j: (0, 0, j)),
        interpret=INTERPRET,
    )(pick_cls, pick_box, ops, window, cosines, sines)


def split_parts(values):
    high = lax.reduce_precision(values, exponent_bits=8, mantissa_bits=7)
    low = values - high
    return jnp.concatenate([high.astype(jnp.bfloat16), low.astype(jnp.bfloat16)], axis=0)


def make_body(box_count, ang_count):
    devices = box_count * ang_count

    def body(
        children, interp_band, band_start, shift_angle, far_box, far_class, far_count, translation
    ):
        high_width = interp_band.shape[0]
        low_width = children.shape[2]
        parents_here = children.shape[0] // 8
        assert parents_here >= REACH
        f32 = jnp.float32
        interp = lax.optimization_barrier(build_interp(interp_band, band_start))
        raised_re = jnp.dot(children[:, 0], interp, preferred_element_type=f32).reshape(-1, 8, high_width)
        raised_im = jnp.dot(children[:, 1], interp, preferred_element_type=f32).reshape(-1, 8, high_width)
        cosines = jnp.cos(shift_angle)
        sines = jnp.sin(shift_angle)
        parent_re = jnp.sum(raised_re * cosines - raised_im * sines, axis=1)
        parent_im = jnp.sum(raised_re * sines + raised_im * cosines, axis=1)
        parent = jnp.stack([parent_re, parent_im]).astype(jnp.bfloat16)
        axes = ("box", "ang")
        up = [(i, i + 1) for i in range(devices - 1)]
        down = [(i + 1, i) for i in range(devices - 1)]
        before = lax.ppermute(parent[:, parents_here - REACH:], axes, up)
        after = lax.ppermute(parent[:, :REACH], axes, down)
        window = jnp.concatenate([before, parent, after], axis=1)
        ang = lax.axis_index("ang")
        device = lax.axis_index("box") * ang_count + ang
        first = ang * parents_here
        my_box = lax.dynamic_slice_in_dim(far_box, first, parents_here, 0)
        my_class = lax.dynamic_slice_in_dim(far_class, first, parents_here, 0)
        my_count = lax.dynamic_slice_in_dim(far_count, first, parents_here, 0)
        rel_box = my_box - (device * parents_here - REACH)
        spread = translate(window, translation, rel_box, my_class, my_count, cosines, sines)
        contract = (((1,), (1,)), ((), ()))
        result = lax.dot_general(
            spread.reshape(-1, high_width), interp, contract, preferred_element_type=f32
        )
        return result.reshape(2, -1, low_width).transpose(1, 0, 2)

    return body


def solution(mesh):
    return jax.shard_map(
        make_body(mesh.shape["box"], mesh.shape["ang"]),
        mesh=mesh,
        in_specs=(
            P(("box", "ang"), None, None),
            P(),
            P(),
            P(),
            P("box", None),
            P("box", None),
            P("box"),
            P(),
        ),
        out_specs=P(("box", "ang"), None, None),
        check_vma=False,
    )
```

```python
import jax
import jax.numpy as jnp
from jax import lax
from jax.sharding import PartitionSpec as P
from jax.experimental import pallas as pl

INTERPRET = False
CHUNK = 512

K_LOW = 1024
REACH = 16


def build_interp(interp_band, band_start):
    offset = jnp.arange(K_LOW, dtype=jnp.int32)[:, None] - band_start[None, :]
    weights = interp_band.T.astype(jnp.bfloat16)
    dense = jnp.zeros((K_LOW, interp_band.shape[0]), jnp.bfloat16)
    for column in range(interp_band.shape[1]):
        dense = jnp.where(offset == column, weights[column][None, :], dense)
    return dense


def translate_kernel(pick_cls_ref, pick_box_ref, ops_ref, win_ref, cos_ref, sin_ref, out_ref):
    f32 = jnp.float32
    pick_cls = pick_cls_ref[...]
    pick_box = pick_box_ref[...]
    t_re = jnp.dot(pick_cls, ops_ref[0], preferred_element_type=f32)
    t_im = jnp.dot(pick_cls, ops_ref[1], preferred_element_type=f32)
    p_re = jnp.dot(pick_box, win_ref[0], preferred_element_type=f32)
    p_im = jnp.dot(pick_box, win_ref[1], preferred_element_type=f32)
    real_part = t_re * p_re - t_im * p_im
    imag_part = t_re * p_im + t_im * p_re
    rows = out_ref.shape[1] // 8
    acc_re = real_part[0:rows]
    acc_im = imag_part[0:rows]
    for slot in range(1, real_part.shape[0] // rows):
        acc_re = acc_re + real_part[slot * rows:(slot + 1) * rows]
        acc_im = acc_im + imag_part[slot * rows:(slot + 1) * rows]
    local_re = acc_re.astype(jnp.bfloat16).astype(f32)[:, None, :]
    local_im = acc_im.astype(jnp.bfloat16).astype(f32)[:, None, :]
    cosines = cos_ref[...][None]
    sines = sin_ref[...][None]
    spread_re = local_re * cosines + local_im * sines
    spread_im = local_im * cosines - local_re * sines
    out_ref[0] = spread_re.reshape(out_ref.shape[1], -1).astype(out_ref.dtype)
    out_ref[1] = spread_im.reshape(out_ref.shape[1], -1).astype(out_ref.dtype)


def translate(window, translation, rel_box, classes, counts, cosines, sines):
    rows, far = classes.shape
    width = window.shape[1]
    nclass = translation.shape[0]
    slots = jnp.arange(far, dtype=jnp.int32)
    live = slots[None, :] < counts[:, None]
    box_t = rel_box.T.reshape(-1)
    cls_t = classes.T.reshape(-1)
    live_t = live.T.reshape(-1)
    pick_box = jnp.logical_and(
        box_t[:, None] == jnp.arange(width, dtype=jnp.int32)[None, :], live_t[:, None]
    ).astype(jnp.bfloat16)
    pick_cls = (cls_t[:, None] == jnp.arange(nclass, dtype=jnp.int32)[None, :]).astype(jnp.bfloat16)
    pick_cls = jnp.concatenate([pick_cls, pick_cls], axis=1)
    ops = split_parts(translation).transpose(1, 0, 2)
    k_high = window.shape[2]
    slots_rows = pick_cls.shape[0]
    return pl.pallas_call(
        translate_kernel,
        out_shape=jax.ShapeDtypeStruct((2, rows * 8, k_high), jnp.bfloat16),
        grid=(k_high // CHUNK,),
        in_specs=[
            pl.BlockSpec((slots_rows, pick_cls.shape[1]), lambda j: (0, 0)),
            pl.BlockSpec((slots_rows, width), lambda j: (0, 0)),
            pl.BlockSpec((2, ops.shape[1], CHUNK), lambda j: (0, 0, j)),
            pl.BlockSpec((2, width, CHUNK), lambda j: (0, 0, j)),
            pl.BlockSpec((8, CHUNK), lambda j: (0, j)),
            pl.BlockSpec((8, CHUNK), lambda j: (0, j)),
        ],
        out_specs=pl.BlockSpec((2, rows * 8, CHUNK), lambda j: (0, 0, j)),
        interpret=INTERPRET,
    )(pick_cls, pick_box, ops, window, cosines, sines)


def split_parts(values):
    high = lax.reduce_precision(values, exponent_bits=8, mantissa_bits=7)
    low = values - high
    return jnp.concatenate([high.astype(jnp.bfloat16), low.astype(jnp.bfloat16)], axis=0)


def make_body(box_count, ang_count):
    devices = box_count * ang_count

    def body(
        children, interp_band, band_start, shift_angle, far_box, far_class, far_count, translation
    ):
        high_width = interp_band.shape[0]
        low_width = children.shape[2]
        parents_here = children.shape[0] // 8
        assert parents_here >= REACH
        f32 = jnp.float32
        interp = lax.optimization_barrier(build_interp(interp_band, band_start))
        raised_re = jnp.dot(children[:, 0], interp, preferred_element_type=f32).reshape(-1, 8, high_width)
        raised_im = jnp.dot(children[:, 1], interp, preferred_element_type=f32).reshape(-1, 8, high_width)
        cosines = jnp.cos(shift_angle)
        sines = jnp.sin(shift_angle)
        parent_re = jnp.sum(raised_re * cosines - raised_im * sines, axis=1)
        parent_im = jnp.sum(raised_re * sines + raised_im * cosines, axis=1)
        parent = jnp.stack([parent_re, parent_im]).astype(jnp.bfloat16)
        axes = ("box", "ang")
        up = [(i, i + 1) for i in range(devices - 1)]
        down = [(i + 1, i) for i in range(devices - 1)]
        before = lax.ppermute(parent[:, parents_here - REACH:], axes, up)
        after = lax.ppermute(parent[:, :REACH], axes, down)
        window = jnp.concatenate([before, parent, after], axis=1)
        ang = lax.axis_index("ang")
        device = lax.axis_index("box") * ang_count + ang
        first = ang * parents_here
        my_box = lax.dynamic_slice_in_dim(far_box, first, parents_here, 0)
        my_class = lax.dynamic_slice_in_dim(far_class, first, parents_here, 0)
        my_count = lax.dynamic_slice_in_dim(far_count, first, parents_here, 0)
        rel_box = my_box - (device * parents_here - REACH)
        spread = translate(window, translation, rel_box, my_class, my_count, cosines, sines)
        contract = (((1,), (1,)), ((), ()))
        result = lax.dot_general(
            spread.reshape(-1, high_width), interp, contract, preferred_element_type=f32
        )
        return result.reshape(2, -1, low_width).transpose(1, 0, 2)

    return body


def solution(mesh):
    return jax.shard_map(
        make_body(mesh.shape["box"], mesh.shape["ang"]),
        mesh=mesh,
        in_specs=(
            P(("box", "ang"), None, None),
            P(),
            P(),
            P(),
            P("box", None),
            P("box", None),
            P("box"),
            P(),
        ),
        out_specs=P(("box", "ang"), None, None),
        check_vma=False,
    )
```

```python
import jax
import jax.numpy as jnp
from jax import lax
from jax.sharding import PartitionSpec as P
from jax.experimental import pallas as pl

INTERPRET = False
CHUNK = 1024

K_LOW = 1024
REACH = 16


def build_interp(interp_band, band_start):
    offset = jnp.arange(K_LOW, dtype=jnp.int32)[:, None] - band_start[None, :]
    weights = interp_band.T
    dense = jnp.zeros((K_LOW, interp_band.shape[0]), jnp.float32)
    for column in range(interp_band.shape[1]):
        dense = jnp.where(offset == column, weights[column][None, :], dense)
    return dense.astype(jnp.bfloat16)


def translate_kernel(pick_cls_ref, pick_box_ref, ops_ref, win_ref, cos_ref, sin_ref, out_ref):
    f32 = jnp.float32
    pick_cls = pick_cls_ref[...]
    pick_box = pick_box_ref[...]
    t_re = jnp.dot(pick_cls, ops_ref[0], preferred_element_type=f32)
    t_im = jnp.dot(pick_cls, ops_ref[1], preferred_element_type=f32)
    p_re = jnp.dot(pick_box, win_ref[0], preferred_element_type=f32)
    p_im = jnp.dot(pick_box, win_ref[1], preferred_element_type=f32)
    real_part = t_re * p_re - t_im * p_im
    imag_part = t_re * p_im + t_im * p_re
    rows = out_ref.shape[1] // 8
    acc_re = real_part[0:rows]
    acc_im = imag_part[0:rows]
    for slot in range(1, real_part.shape[0] // rows):
        acc_re = acc_re + real_part[slot * rows:(slot + 1) * rows]
        acc_im = acc_im + imag_part[slot * rows:(slot + 1) * rows]
    local_re = acc_re.astype(jnp.bfloat16).astype(f32)[:, None, :]
    local_im = acc_im.astype(jnp.bfloat16).astype(f32)[:, None, :]
    cosines = cos_ref[...][None]
    sines = sin_ref[...][None]
    spread_re = local_re * cosines + local_im * sines
    spread_im = local_im * cosines - local_re * sines
    out_ref[0] = spread_re.reshape(out_ref.shape[1], -1).astype(out_ref.dtype)
    out_ref[1] = spread_im.reshape(out_ref.shape[1], -1).astype(out_ref.dtype)


def translate(window, translation, rel_box, classes, counts, cosines, sines):
    rows, far = classes.shape
    width = window.shape[1]
    nclass = translation.shape[0]
    slots = jnp.arange(far, dtype=jnp.int32)
    live = slots[None, :] < counts[:, None]
    box_t = rel_box.T.reshape(-1)
    cls_t = classes.T.reshape(-1)
    live_t = live.T.reshape(-1)
    pick_box = jnp.logical_and(
        box_t[:, None] == jnp.arange(width, dtype=jnp.int32)[None, :], live_t[:, None]
    ).astype(jnp.bfloat16)
    pick_cls = (cls_t[:, None] == jnp.arange(nclass, dtype=jnp.int32)[None, :]).astype(jnp.bfloat16)
    pick_cls = jnp.concatenate([pick_cls, pick_cls], axis=1)
    ops = split_parts(translation).transpose(1, 0, 2)
    k_high = window.shape[2]
    slots_rows = pick_cls.shape[0]
    return pl.pallas_call(
        translate_kernel,
        out_shape=jax.ShapeDtypeStruct((2, rows * 8, k_high), jnp.bfloat16),
        grid=(k_high // CHUNK,),
        in_specs=[
            pl.BlockSpec((slots_rows, pick_cls.shape[1]), lambda j: (0, 0)),
            pl.BlockSpec((slots_rows, width), lambda j: (0, 0)),
            pl.BlockSpec((2, ops.shape[1], CHUNK), lambda j: (0, 0, j)),
            pl.BlockSpec((2, width, CHUNK), lambda j: (0, 0, j)),
            pl.BlockSpec((8, CHUNK), lambda j: (0, j)),
            pl.BlockSpec((8, CHUNK), lambda j: (0, j)),
        ],
        out_specs=pl.BlockSpec((2, rows * 8, CHUNK), lambda j: (0, 0, j)),
        interpret=INTERPRET,
    )(pick_cls, pick_box, ops, window, cosines, sines)


def split_parts(values):
    high = lax.reduce_precision(values, exponent_bits=8, mantissa_bits=7)
    low = values - high
    return jnp.concatenate([high.astype(jnp.bfloat16), low.astype(jnp.bfloat16)], axis=0)


def make_body(box_count, ang_count):
    devices = box_count * ang_count

    def body(
        children, interp_band, band_start, shift_angle, far_box, far_class, far_count, translation
    ):
        high_width = interp_band.shape[0]
        low_width = children.shape[2]
        parents_here = children.shape[0] // 8
        assert parents_here >= REACH
        f32 = jnp.float32
        interp = lax.optimization_barrier(build_interp(interp_band, band_start))
        raised_re = jnp.dot(children[:, 0], interp, preferred_element_type=f32).reshape(-1, 8, high_width)
        raised_im = jnp.dot(children[:, 1], interp, preferred_element_type=f32).reshape(-1, 8, high_width)
        cosines = jnp.cos(shift_angle)
        sines = jnp.sin(shift_angle)
        parent_re = jnp.sum(raised_re * cosines - raised_im * sines, axis=1)
        parent_im = jnp.sum(raised_re * sines + raised_im * cosines, axis=1)
        parent = jnp.stack([parent_re, parent_im]).astype(jnp.bfloat16)
        axes = ("box", "ang")
        up = [(i, i + 1) for i in range(devices - 1)]
        down = [(i + 1, i) for i in range(devices - 1)]
        before = lax.ppermute(parent[:, parents_here - REACH:], axes, up)
        after = lax.ppermute(parent[:, :REACH], axes, down)
        window = jnp.concatenate([before, parent, after], axis=1)
        ang = lax.axis_index("ang")
        device = lax.axis_index("box") * ang_count + ang
        first = ang * parents_here
        my_box = lax.dynamic_slice_in_dim(far_box, first, parents_here, 0)
        my_class = lax.dynamic_slice_in_dim(far_class, first, parents_here, 0)
        my_count = lax.dynamic_slice_in_dim(far_count, first, parents_here, 0)
        rel_box = my_box - (device * parents_here - REACH)
        spread = translate(window, translation, rel_box, my_class, my_count, cosines, sines)
        contract = (((1,), (1,)), ((), ()))
        result = lax.dot_general(
            spread.reshape(-1, high_width), interp, contract, preferred_element_type=f32
        )
        return result.reshape(2, -1, low_width).transpose(1, 0, 2)

    return body


def solution(mesh):
    return jax.shard_map(
        make_body(mesh.shape["box"], mesh.shape["ang"]),
        mesh=mesh,
        in_specs=(
            P(("box", "ang"), None, None),
            P(),
            P(),
            P(),
            P("box", None),
            P("box", None),
            P("box"),
            P(),
        ),
        out_specs=P(("box", "ang"), None, None),
        check_vma=False,
    )
```

```python
import jax
import jax.numpy as jnp
from jax import lax
from jax.sharding import PartitionSpec as P
from jax.experimental import pallas as pl

INTERPRET = False
CHUNK = 2048

K_LOW = 1024
REACH = 16


def build_interp(interp_band, band_start):
    offset = jnp.arange(K_LOW, dtype=jnp.int32)[:, None] - band_start[None, :]
    weights = interp_band.T
    dense = jnp.zeros((K_LOW, interp_band.shape[0]), jnp.float32)
    for column in range(interp_band.shape[1]):
        dense = jnp.where(offset == column, weights[column][None, :], dense)
    return dense.astype(jnp.bfloat16)


def translate_kernel(pick_cls_ref, pick_box_ref, ops_ref, win_ref, cos_ref, sin_ref, out_ref):
    f32 = jnp.float32
    pick_cls = pick_cls_ref[...]
    pick_box = pick_box_ref[...]
    t_re = jnp.dot(pick_cls, ops_ref[0], preferred_element_type=f32)
    t_im = jnp.dot(pick_cls, ops_ref[1], preferred_element_type=f32)
    p_re = jnp.dot(pick_box, win_ref[0], preferred_element_type=f32)
    p_im = jnp.dot(pick_box, win_ref[1], preferred_element_type=f32)
    real_part = t_re * p_re - t_im * p_im
    imag_part = t_re * p_im + t_im * p_re
    rows = out_ref.shape[1] // 8
    acc_re = real_part[0:rows]
    acc_im = imag_part[0:rows]
    for slot in range(1, real_part.shape[0] // rows):
        acc_re = acc_re + real_part[slot * rows:(slot + 1) * rows]
        acc_im = acc_im + imag_part[slot * rows:(slot + 1) * rows]
    local_re = acc_re.astype(jnp.bfloat16).astype(f32)[:, None, :]
    local_im = acc_im.astype(jnp.bfloat16).astype(f32)[:, None, :]
    cosines = cos_ref[...][None]
    sines = sin_ref[...][None]
    spread_re = local_re * cosines + local_im * sines
    spread_im = local_im * cosines - local_re * sines
    out_ref[0] = spread_re.reshape(out_ref.shape[1], -1).astype(out_ref.dtype)
    out_ref[1] = spread_im.reshape(out_ref.shape[1], -1).astype(out_ref.dtype)


def translate(window, translation, rel_box, classes, counts, cosines, sines):
    rows, far = classes.shape
    width = window.shape[1]
    nclass = translation.shape[0]
    slots = jnp.arange(far, dtype=jnp.int32)
    live = slots[None, :] < counts[:, None]
    box_t = rel_box.T.reshape(-1)
    cls_t = classes.T.reshape(-1)
    live_t = live.T.reshape(-1)
    pick_box = jnp.logical_and(
        box_t[:, None] == jnp.arange(width, dtype=jnp.int32)[None, :], live_t[:, None]
    ).astype(jnp.bfloat16)
    pick_cls = (cls_t[:, None] == jnp.arange(nclass, dtype=jnp.int32)[None, :]).astype(jnp.bfloat16)
    pick_cls = jnp.concatenate([pick_cls, pick_cls], axis=1)
    ops = split_parts(translation).transpose(1, 0, 2)
    k_high = window.shape[2]
    slots_rows = pick_cls.shape[0]
    return pl.pallas_call(
        translate_kernel,
        out_shape=jax.ShapeDtypeStruct((2, rows * 8, k_high), jnp.bfloat16),
        grid=(k_high // CHUNK,),
        in_specs=[
            pl.BlockSpec((slots_rows, pick_cls.shape[1]), lambda j: (0, 0)),
            pl.BlockSpec((slots_rows, width), lambda j: (0, 0)),
            pl.BlockSpec((2, ops.shape[1], CHUNK), lambda j: (0, 0, j)),
            pl.BlockSpec((2, width, CHUNK), lambda j: (0, 0, j)),
            pl.BlockSpec((8, CHUNK), lambda j: (0, j)),
            pl.BlockSpec((8, CHUNK), lambda j: (0, j)),
        ],
        out_specs=pl.BlockSpec((2, rows * 8, CHUNK), lambda j: (0, 0, j)),
        interpret=INTERPRET,
    )(pick_cls, pick_box, ops, window, cosines, sines)


def split_parts(values):
    high = lax.reduce_precision(values, exponent_bits=8, mantissa_bits=7)
    low = values - high
    return jnp.concatenate([high.astype(jnp.bfloat16), low.astype(jnp.bfloat16)], axis=0)


def make_body(box_count, ang_count):
    devices = box_count * ang_count

    def body(
        children, interp_band, band_start, shift_angle, far_box, far_class, far_count, translation
    ):
        high_width = interp_band.shape[0]
        low_width = children.shape[2]
        parents_here = children.shape[0] // 8
        assert parents_here >= REACH
        f32 = jnp.float32
        interp = lax.optimization_barrier(build_interp(interp_band, band_start))
        raised_re = jnp.dot(children[:, 0], interp, preferred_element_type=f32).reshape(-1, 8, high_width)
        raised_im = jnp.dot(children[:, 1], interp, preferred_element_type=f32).reshape(-1, 8, high_width)
        cosines = jnp.cos(shift_angle)
        sines = jnp.sin(shift_angle)
        parent_re = jnp.sum(raised_re * cosines - raised_im * sines, axis=1)
        parent_im = jnp.sum(raised_re * sines + raised_im * cosines, axis=1)
        parent = jnp.stack([parent_re, parent_im]).astype(jnp.bfloat16)
        axes = ("box", "ang")
        up = [(i, i + 1) for i in range(devices - 1)]
        down = [(i + 1, i) for i in range(devices - 1)]
        before = lax.ppermute(parent[:, parents_here - REACH:], axes, up)
        after = lax.ppermute(parent[:, :REACH], axes, down)
        window = jnp.concatenate([before, parent, after], axis=1)
        ang = lax.axis_index("ang")
        device = lax.axis_index("box") * ang_count + ang
        first = ang * parents_here
        my_box = lax.dynamic_slice_in_dim(far_box, first, parents_here, 0)
        my_class = lax.dynamic_slice_in_dim(far_class, first, parents_here, 0)
        my_count = lax.dynamic_slice_in_dim(far_count, first, parents_here, 0)
        rel_box = my_box - (device * parents_here - REACH)
        spread = translate(window, translation, rel_box, my_class, my_count, cosines, sines)
        contract = (((1,), (1,)), ((), ()))
        result = lax.dot_general(
            spread.reshape(-1, high_width), interp, contract, preferred_element_type=f32
        )
        return result.reshape(2, -1, low_width).transpose(1, 0, 2)

    return body


def solution(mesh):
    return jax.shard_map(
        make_body(mesh.shape["box"], mesh.shape["ang"]),
        mesh=mesh,
        in_specs=(
            P(("box", "ang"), None, None),
            P(),
            P(),
            P(),
            P("box", None),
            P("box", None),
            P("box"),
            P(),
        ),
        out_specs=P(("box", "ang"), None, None),
        check_vma=False,
    )
```
